256 devices in a mesh: batch: 8 (over z), replica: 32 (over y, x, core).
Axes of the slice: x: 4, y: 4, z: 8, core: 2. Of those that a mesh axis runs over, the one named last changes fastest.
Arguments:
- patches: bfloat16 [32, 64, 64, 1024], P('replica', 'batch'), may hold values from -6 to 6
- visible_order: int32 [32, 64, 64], P('replica', 'batch'), may hold values from 0 to 63, each once within a row
- visible_counts: int32 [32, 64], P('replica'), may hold values from 1 to 32, as said below
- dest_rows: int32 [32, 64], P('replica'), may hold values from 0 to 1023, as said below
- qkv_weight: bfloat16 [1024, 3072], P('replica')
- out_weight: bfloat16 [1024, 1024], P('replica'), may hold values from -0.1875 to 0.1875
- norm_gain: bfloat16 [1024], P('replica'), may hold values from 0.5 to 1.5
- upstream: bfloat16 [32, 1024, 1024], P('replica', 'batch'), may hold values from -6 to 6
Outputs:
- layer_out: bfloat16 [32, 1024, 1024], P('replica', 'batch')
- d_packed: bfloat16 [32, 1024, 1024], P('replica', 'batch')
- grad_qkv: float32 [1024, 3072], P('replica')
- grad_out: float32 [1024, 1024], P('replica')
- grad_gain: float32 [1024], P('replica')
The draws below stay inside these ranges and needn't reach their ends.
Inputs may be any that keep to these rules, and one draw needn't show every extreme that they name: `visible_counts`: in every replica index, each batch index b packs exactly 128 rows: the volumes with dest_rows // 128 == b, one from every device of the batch axis, in order of that device's batch index, without gaps; one of them has 32 visible patches. `dest_rows`: the 8 volumes of one device go to 8 different batch indices; a volume's rows never cross a multiple of 128.
All inputs are finite; a program needn't handle non-finite values.
Results may differ from the reference program's by a relative error of at most 0.033.
Values may be sent and summed in bfloat16 or wider, within the bound.
No kernel may reach another device: no remote copies, remote signals or barrier semaphores. Data moves between devices by JAX's collectives and lax.ppermute only.
A program may use at most 128 MiB of HBM per device.

```python
import jax
import jax.numpy as jnp
from jax import lax

D = 1024
HEADS = 16
P_SIZE = 64
MAXVIS = 32
VOL_DEV = 8
GROUP_VOLS = 64
CAP = 128
PACKED = 1024
REPLICAS = 32


def layout_tables(key):
    base = jax.random.fold_in(key, 11)
    keys = jax.random.split(base, 5)
    width = VOL_DEV
    first = jax.random.randint(keys[0], (REPLICAS, width, 1), 1, MAXVIS // 2)
    second = jax.random.randint(keys[1], (REPLICAS, width, 1), 1, MAXVIS // 2)
    largest = jnp.full((REPLICAS, width, 1), MAXVIS, jnp.int32)
    leading = jnp.concatenate([largest, first, second, MAXVIS - first - second], axis=-1)
    pair_low = jax.random.randint(keys[2], (REPLICAS, width, (width - 4) // 2), 1, MAXVIS)
    pairs = jnp.stack([pair_low, MAXVIS - pair_low], axis=-1).reshape(REPLICAS, width, width - 4)
    lengths = jnp.concatenate([leading, pairs], axis=-1)
    scores = jax.random.randint(keys[3], (REPLICAS, width, width), 0, 1 << 20) * width + jnp.arange(width, dtype=jnp.int32)
    shuffle = jnp.argsort(scores, axis=-1)
    by_source = jnp.take_along_axis(lengths, shuffle, axis=-1)
    starts = jnp.cumsum(by_source, axis=-1) - by_source
    shifts = jax.random.randint(keys[4], (REPLICAS, width, 1), 0, width)
    target = (jnp.arange(width, dtype=jnp.int32)[None, None, :] + shifts) % width
    counts = jnp.take_along_axis(jnp.transpose(by_source, (0, 2, 1)), target, axis=-1)
    begins = jnp.take_along_axis(jnp.transpose(starts, (0, 2, 1)), target, axis=-1)
    rows = target * CAP + begins
    return (counts.reshape(REPLICAS, GROUP_VOLS).astype(jnp.int32), rows.reshape(REPLICAS, GROUP_VOLS).astype(jnp.int32))


def draw_visible_counts(key, part):
    return layout_tables(key)[0]


def draw_dest_rows(key, part):
    return layout_tables(key)[1]


def draw_qkv_weight(key, part):
    base = jax.random.normal(jax.random.fold_in(key, 3), (D, 3 * D), jnp.float32) * D ** (-0.5)
    return base.astype(jnp.bfloat16)


def level_of(stream_key, dims, cuts, least, high):
    def one(position, parts):
        heights = jax.random.uniform(jax.random.fold_in(jax.random.fold_in(stream_key, 6), position), (parts,), jnp.float32, least / len(cuts), high / len(cuts))
        return jnp.repeat(jnp.exp(heights), dims[position] // parts).reshape((-1,) + (1,) * (len(dims) - position - 1))

    level = one(*cuts[0])
    for cut in cuts[1:]:
        level = level * one(*cut)
    return level


def bell_draw(stream_key, shape, scale, limit, cuts=(), kind=jnp.bfloat16):
    level = level_of(stream_key, shape, cuts, -0.22, 0.18) if cuts else 1.0
    array = jax.random.normal(stream_key, shape, jnp.float32) * scale * level
    return jnp.minimum(jnp.maximum(array, -limit), limit).astype(kind)


def setup_inputs(seed: int = 0) -> dict:
    key_list = jax.random.split(jax.random.key(seed), 9)
    patches = bell_draw(key_list[0], (REPLICAS, GROUP_VOLS, P_SIZE, D), 1.0, 6.0, ((0, 32), (1, 8)))
    visible_order = jax.vmap(lambda own: jax.random.permutation(own, P_SIZE))(jax.random.split(key_list[1], REPLICAS * GROUP_VOLS)).reshape((REPLICAS, GROUP_VOLS, P_SIZE)).astype(jnp.int32)
    visible_counts = draw_visible_counts(jax.random.fold_in(key_list[8], 71), 0)
    dest_rows = draw_dest_rows(jax.random.fold_in(key_list[8], 71), 0)
    qkv_weight = draw_qkv_weight(jax.random.fold_in(key_list[8], 71), 0)
    out_weight = bell_draw(key_list[5], (D, D), D ** -0.5, 0.1875, ((0, 32),))
    norm_gain = jnp.clip(1.0 + 0.1 * jax.random.normal(key_list[6], (D,), jnp.float32), 0.5, 1.5).astype(jnp.bfloat16)
    upstream = bell_draw(key_list[7], (REPLICAS, PACKED, D), 1.0, 6.0, ((0, 32), (1, 8)))
    return {"patches": patches, "visible_order": visible_order, "visible_counts": visible_counts, "dest_rows": dest_rows, "qkv_weight": qkv_weight, "out_weight": out_weight, "norm_gain": norm_gain, "upstream": upstream}


EPS = 1e-06
NEG = -1e+30

def layer_core(tokens, upward, allowed, wqkv, wout, gain):
    groups, length, width = tokens.shape
    rows = groups * length
    head_dim = width // HEADS
    scale = head_dim ** (-0.5)
    x32 = tokens.astype(jnp.float32).reshape(rows, width)
    row_average = lax.optimization_barrier(jnp.mean(x32, axis=1, keepdims=True))
    centered_rows = x32 - row_average
    inverse_deviation = lax.rsqrt(lax.optimization_barrier(jnp.mean(centered_rows * centered_rows, axis=1, keepdims=True)) + EPS)
    standardized_rows = centered_rows * inverse_deviation
    gain_float32 = gain.astype(jnp.float32)
    layernorm_output = (standardized_rows * gain_float32).astype(jnp.bfloat16)
    qkv = jnp.dot(layernorm_output, wqkv, preferred_element_type=jnp.float32).astype(jnp.bfloat16)
    query = qkv[:, :width].reshape(groups, length, HEADS, head_dim).astype(jnp.float32)
    keys = qkv[:, width:2 * width].reshape(groups, length, HEADS, head_dim).astype(jnp.float32)
    values = qkv[:, 2 * width:].reshape(groups, length, HEADS, head_dim).astype(jnp.float32)
    scores = jnp.einsum('gqhd,gkhd->ghqk', query, keys) * scale
    scores = jnp.where(allowed[:, None], scores, NEG)
    top = lax.optimization_barrier(jnp.max(scores, axis=-1, keepdims=True))
    expd = jnp.exp(scores - top)
    probs = expd / lax.optimization_barrier(jnp.sum(expd, axis=-1, keepdims=True))
    weights = probs.astype(jnp.bfloat16)
    context = jnp.einsum('ghqk,gkhd->gqhd', weights.astype(jnp.float32), values).astype(jnp.bfloat16).reshape(rows, width)
    result = (x32 + jnp.dot(context, wout, preferred_element_type=jnp.float32)).astype(jnp.bfloat16)
    up_rows = upward.reshape(rows, width)
    d_context = jnp.dot(up_rows, wout.T, preferred_element_type=jnp.float32).astype(jnp.bfloat16)
    d_context = d_context.reshape(groups, length, HEADS, head_dim).astype(jnp.float32)
    d_values = jnp.einsum('ghqk,gqhd->gkhd', weights.astype(jnp.float32), d_context).astype(jnp.bfloat16)
    d_weights = jnp.einsum('gqhd,gkhd->ghqk', d_context, values)
    d_scores = (probs * (d_weights - lax.optimization_barrier(jnp.sum(d_weights * probs, axis=-1, keepdims=True))) * scale).astype(jnp.bfloat16)
    d_query = jnp.einsum('ghqk,gkhd->gqhd', d_scores.astype(jnp.float32), keys).astype(jnp.bfloat16)
    d_keys = jnp.einsum('ghqk,gqhd->gkhd', d_scores.astype(jnp.float32), query).astype(jnp.bfloat16)
    d_qkv = jnp.concatenate([d_query.reshape(rows, width), d_keys.reshape(rows, width), d_values.reshape(rows, width)], axis=1)
    layernorm_gradient = jnp.dot(d_qkv, wqkv.T, preferred_element_type=jnp.float32)
    gain_products = lax.optimization_barrier(jnp.sum(layernorm_gradient * standardized_rows, axis=0))
    normalized_gradient = layernorm_gradient * gain_float32
    input_gradient = inverse_deviation * (normalized_gradient - lax.optimization_barrier(jnp.mean(normalized_gradient, axis=1, keepdims=True)) - standardized_rows * lax.optimization_barrier(jnp.mean(normalized_gradient * standardized_rows, axis=1, keepdims=True)))
    d_tokens = (up_rows.astype(jnp.float32) + input_gradient).astype(jnp.bfloat16)
    return (result.reshape(tokens.shape), d_tokens.reshape(tokens.shape), layernorm_output, context, d_qkv, up_rows, gain_products)

def reference(patches, visible_order, visible_counts, dest_rows, qkv_weight, out_weight, norm_gain, upstream):
    slot = jnp.arange(MAXVIS, dtype=jnp.int32)

    def group_step(totals, inputs):
        vol_patches, order, counts, starts, upward_packed = inputs
        picked = jnp.take_along_axis(vol_patches, order[:, :MAXVIS, None].astype(jnp.int32), axis=1)
        valid = slot[None, :] < counts[:, None]
        allowed = jnp.broadcast_to(valid[:, None, :], (GROUP_VOLS, MAXVIS, MAXVIS))
        where_rows = (starts[:, None] + slot[None, :]).astype(jnp.int32)
        clipped = jnp.clip(where_rows, 0, PACKED - 1)
        gathered = jnp.take(upward_packed, clipped.reshape(-1), axis=0).reshape(GROUP_VOLS, MAXVIS, D)
        upward = jnp.where(valid[..., None], gathered, jnp.zeros_like(gathered))
        result, d_tokens, layernorm_output, context, d_qkv, up_rows, gain_products = layer_core(picked, upward, allowed, qkv_weight, out_weight, norm_gain)
        target = jnp.where(valid, where_rows, PACKED).reshape(-1)
        packed_out = jnp.zeros((PACKED, D), jnp.bfloat16).at[target].set(result.reshape(-1, D), mode='drop')
        packed_grad = jnp.zeros((PACKED, D), jnp.bfloat16).at[target].set(d_tokens.reshape(-1, D), mode='drop')
        totals = (totals[0] + jnp.dot(layernorm_output.T, d_qkv, preferred_element_type=jnp.float32), totals[1] + jnp.dot(context.T, up_rows, preferred_element_type=jnp.float32), totals[2] + gain_products)
        return (totals, (packed_out, packed_grad))
    start = (jnp.zeros((D, 3 * D), jnp.float32), jnp.zeros((D, D), jnp.float32), jnp.zeros((D,), jnp.float32))
    totals, packed = lax.scan(group_step, start, (patches, visible_order, visible_counts, dest_rows, upstream))
    return (packed[0], packed[1], totals[0], totals[1], totals[2])
```

```python
import jax
import jax.numpy as jnp
from jax import lax
from jax.sharding import PartitionSpec as P

HEADS = 16
MAXVIS = 32
MEANVIS = 16


EPS = 1e-06
NEG = -1e30


def layer_core(tokens, upward, allowed, wqkv, wout, gain):
    groups, length, width = tokens.shape
    rows = groups * length
    head_dim = width // HEADS
    scale = head_dim ** (-0.5)
    x32 = tokens.astype(jnp.float32).reshape(rows, width)
    row_average = jnp.mean(x32, axis=1, keepdims=True)
    centered_rows = x32 - row_average
    inverse_deviation = lax.rsqrt(
        jnp.mean(centered_rows * centered_rows, axis=1, keepdims=True) + EPS
    )
    standardized_rows = centered_rows * inverse_deviation
    gain_float32 = gain.astype(jnp.float32)
    layernorm_output = (standardized_rows * gain_float32).astype(jnp.bfloat16)
    qkv = jnp.dot(layernorm_output, wqkv, preferred_element_type=jnp.float32).astype(jnp.bfloat16)
    query = qkv[:, :width].reshape(groups, length, HEADS, head_dim)
    keys = qkv[:, width : 2 * width].reshape(groups, length, HEADS, head_dim)
    values = qkv[:, 2 * width :].reshape(groups, length, HEADS, head_dim)
    scores = jnp.einsum("gqhd,gkhd->ghqk", query, keys, preferred_element_type=jnp.float32) * scale
    scores = jnp.where(allowed[:, None], scores, NEG)
    top = jnp.max(scores, axis=-1, keepdims=True)
    expd = jnp.exp(scores - top)
    probs = expd / jnp.sum(expd, axis=-1, keepdims=True)
    weights = probs.astype(jnp.bfloat16)
    context = (
        jnp.einsum("ghqk,gkhd->gqhd", weights, values, preferred_element_type=jnp.float32)
        .astype(jnp.bfloat16)
        .reshape(rows, width)
    )
    result = (x32 + jnp.dot(context, wout, preferred_element_type=jnp.float32)).astype(jnp.bfloat16)
    up_rows = upward.reshape(rows, width)
    d_context = lax.dot_general(
        up_rows, wout, (((1,), (1,)), ((), ())), preferred_element_type=jnp.float32
    ).astype(jnp.bfloat16)
    d_context = d_context.reshape(groups, length, HEADS, head_dim)
    d_values = jnp.einsum(
        "ghqk,gqhd->gkhd", weights, d_context, preferred_element_type=jnp.float32
    ).astype(jnp.bfloat16)
    d_weights = jnp.einsum("gqhd,gkhd->ghqk", d_context, values, preferred_element_type=jnp.float32)
    d_scores = (
        probs * (d_weights - jnp.sum(d_weights * probs, axis=-1, keepdims=True)) * scale
    ).astype(jnp.bfloat16)
    d_query = jnp.einsum(
        "ghqk,gkhd->gqhd", d_scores, keys, preferred_element_type=jnp.float32
    ).astype(jnp.bfloat16)
    d_keys = jnp.einsum(
        "ghqk,gqhd->gkhd", d_scores, query, preferred_element_type=jnp.float32
    ).astype(jnp.bfloat16)
    d_qkv = jnp.concatenate(
        [d_query.reshape(rows, width), d_keys.reshape(rows, width), d_values.reshape(rows, width)],
        axis=1,
    )
    layernorm_gradient = lax.dot_general(
        d_qkv, wqkv, (((1,), (1,)), ((), ())), preferred_element_type=jnp.float32
    )
    gain_products = jnp.sum(layernorm_gradient * standardized_rows, axis=0)
    normalized_gradient = layernorm_gradient * gain_float32
    input_gradient = inverse_deviation * (
        normalized_gradient
        - jnp.mean(normalized_gradient, axis=1, keepdims=True)
        - standardized_rows
        * jnp.mean(normalized_gradient * standardized_rows, axis=1, keepdims=True)
    )
    d_tokens = (up_rows.astype(jnp.float32) + input_gradient).astype(jnp.bfloat16)
    return (
        result.reshape(tokens.shape),
        d_tokens.reshape(tokens.shape),
        layernorm_output,
        context,
        d_qkv,
        up_rows,
        gain_products,
    )


def left_product(left, right):
    return lax.dot_general(
        left, right, (((0,), (0,)), ((), ())), preferred_element_type=jnp.float32
    )


def on_device(
    patches, visible_order, visible_counts, dest_rows, qkv_weight, out_weight, norm_gain, upstream
):
    qkv_cols = qkv_weight.shape[1]
    out_cols = out_weight.shape[1]
    gain_block = jnp.broadcast_to(norm_gain[:, None], (norm_gain.shape[0], 128))
    gathered = lax.all_gather(
        jnp.concatenate([qkv_weight, out_weight, gain_block], axis=1), "replica", axis=0, tiled=True
    )
    wqkv = gathered[:, :qkv_cols]
    wout = gathered[:, qkv_cols : qkv_cols + out_cols]
    gain = gathered[:, qkv_cols + out_cols]
    batches = lax.axis_size("batch")
    me_index = lax.axis_index("batch")
    cap = MEANVIS * batches
    width = wout.shape[1]
    slot = jnp.arange(MAXVIS, dtype=jnp.int32)
    sources = jnp.arange(batches, dtype=jnp.int32)
    counts_all = visible_counts[0].reshape(batches, batches)
    rows_all = dest_rows[0].reshape(batches, batches)
    mine = rows_all // cap == me_index
    src_count = jnp.sum(jnp.where(mine, counts_all, 0), axis=1)
    src_start = jnp.sum(jnp.where(mine, rows_all % cap, 0), axis=1)
    position = jnp.arange(cap, dtype=jnp.int32)
    hit = (position[:, None] >= src_start[None, :]) & (
        position[:, None] < (src_start + src_count)[None, :]
    )
    segment = jnp.sum(jnp.where(hit, sources[None, :], 0), axis=1)
    inside = jnp.sum(jnp.where(hit, position[:, None] - src_start[None, :], 0), axis=1)
    flat_rows = segment * MAXVIS + inside
    my_targets = jnp.take(rows_all, me_index, axis=0) // cap
    to_target = jnp.sum(
        jnp.where(my_targets[None, :] == sources[:, None], sources[None, :], 0), axis=1
    )
    my_counts = jnp.take(counts_all, me_index, axis=0)
    local_rows = jnp.take_along_axis(patches[0], visible_order[0, :, :MAXVIS, None], axis=1)
    live = slot[None, :] < src_count[:, None]
    pick = jnp.clip(src_start[:, None] + slot[None, :], 0, cap - 1)
    fetched = jnp.take(upstream[0], pick.reshape(-1), axis=0).reshape(batches, MAXVIS, width)
    backward_rows = jnp.where(live[..., None], fetched, jnp.zeros_like(fetched))
    returned = lax.all_to_all(backward_rows, "batch", split_axis=0, concat_axis=0, tiled=True)
    upward = jnp.take(returned, my_targets, axis=0)
    valid = slot[None, :] < my_counts[:, None]
    allowed = jnp.broadcast_to(valid[:, None, :], (batches, MAXVIS, MAXVIS))
    result, d_tokens, layernorm_output, context, d_qkv, up_rows, gain_products = layer_core(
        local_rows, upward, allowed, wqkv, wout, gain
    )
    came = lax.all_to_all(
        jnp.take(jnp.concatenate([result, d_tokens], axis=-1), to_target, axis=0),
        "batch",
        split_axis=0,
        concat_axis=0,
        tiled=True,
    )
    came_out = came[..., :width]
    came_grad = came[..., width:]
    layer_out = jnp.take(came_out.reshape(batches * MAXVIS, width), flat_rows, axis=0)
    d_packed = jnp.take(came_grad.reshape(batches * MAXVIS, width), flat_rows, axis=0)
    partial = jnp.concatenate(
        [
            left_product(layernorm_output, d_qkv).astype(jnp.bfloat16),
            left_product(context, up_rows).astype(jnp.bfloat16),
            jnp.broadcast_to(gain_products.astype(jnp.bfloat16)[:, None], (width, 128)),
        ],
        axis=1,
    )
    summed = lax.psum_scatter(partial, "replica", scatter_dimension=0, tiled=True)
    summed = lax.psum(summed, "batch").astype(jnp.float32)
    grad_q = summed[:, :qkv_cols]
    grad_o = summed[:, qkv_cols : qkv_cols + out_cols]
    grad_g = summed[:, qkv_cols + out_cols]
    return (layer_out[None], d_packed[None], grad_q, grad_o, grad_g)


def solution(mesh):
    placed = (
        P("replica", "batch", None, None),
        P("replica", "batch", None),
        P("replica", None),
        P("replica", None),
        P("replica", None),
        P("replica", None),
        P("replica"),
        P("replica", "batch", None),
    )
    return jax.shard_map(
        on_device,
        mesh=mesh,
        in_specs=placed,
        out_specs=(
            P("replica", "batch", None),
            P("replica", "batch", None),
            P("replica", None),
            P("replica", None),
            P("replica"),
        ),
        check_vma=False,
    )
```

```python
import jax
import jax.numpy as jnp
from jax import lax
from jax.sharding import PartitionSpec as P

HEADS = 16
MAXVIS = 32
MEANVIS = 16


EPS = 1e-06
NEG = -1e30


def layer_core(tokens, upward, allowed, wqkv, wout, gain):
    groups, length, width = tokens.shape
    rows = groups * length
    head_dim = width // HEADS
    scale = head_dim ** (-0.5)
    x32 = tokens.astype(jnp.float32).reshape(rows, width)
    row_average = jnp.mean(x32, axis=1, keepdims=True)
    centered_rows = x32 - row_average
    inverse_deviation = lax.rsqrt(
        jnp.mean(centered_rows * centered_rows, axis=1, keepdims=True) + EPS
    )
    standardized_rows = centered_rows * inverse_deviation
    gain_float32 = gain.astype(jnp.float32)
    layernorm_output = (standardized_rows * gain_float32).astype(jnp.bfloat16)
    qkv = jnp.dot(layernorm_output, wqkv, preferred_element_type=jnp.float32).astype(jnp.bfloat16)
    query = qkv[:, :width].reshape(groups, length, HEADS, head_dim)
    keys = qkv[:, width : 2 * width].reshape(groups, length, HEADS, head_dim)
    values = qkv[:, 2 * width :].reshape(groups, length, HEADS, head_dim)
    scores = jnp.einsum("gqhd,gkhd->ghqk", query, keys, preferred_element_type=jnp.float32) * scale
    scores = jnp.where(allowed[:, None], scores, NEG)
    top = jnp.max(scores, axis=-1, keepdims=True)
    expd = jnp.exp(scores - top)
    probs = expd / jnp.sum(expd, axis=-1, keepdims=True)
    weights = probs.astype(jnp.bfloat16)
    context = (
        jnp.einsum("ghqk,gkhd->gqhd", weights, values, preferred_element_type=jnp.float32)
        .astype(jnp.bfloat16)
        .reshape(rows, width)
    )
    result = (x32 + jnp.dot(context, wout, preferred_element_type=jnp.float32)).astype(jnp.bfloat16)
    up_rows = upward.reshape(rows, width)
    d_context = lax.dot_general(
        up_rows, wout, (((1,), (1,)), ((), ())), preferred_element_type=jnp.float32
    ).astype(jnp.bfloat16)
    d_context = d_context.reshape(groups, length, HEADS, head_dim)
    d_values = jnp.einsum(
        "ghqk,gqhd->gkhd", weights, d_context, preferred_element_type=jnp.float32
    ).astype(jnp.bfloat16)
    d_weights = jnp.einsum("gqhd,gkhd->ghqk", d_context, values, preferred_element_type=jnp.float32)
    d_scores = (
        probs * (d_weights - jnp.sum(d_weights * probs, axis=-1, keepdims=True)) * scale
    ).astype(jnp.bfloat16)
    d_query = jnp.einsum(
        "ghqk,gkhd->gqhd", d_scores, keys, preferred_element_type=jnp.float32
    ).astype(jnp.bfloat16)
    d_keys = jnp.einsum(
        "ghqk,gqhd->gkhd", d_scores, query, preferred_element_type=jnp.float32
    ).astype(jnp.bfloat16)
    d_qkv = jnp.concatenate(
        [d_query.reshape(rows, width), d_keys.reshape(rows, width), d_values.reshape(rows, width)],
        axis=1,
    )
    layernorm_gradient = lax.dot_general(
        d_qkv, wqkv, (((1,), (1,)), ((), ())), preferred_element_type=jnp.float32
    )
    gain_products = jnp.sum(layernorm_gradient * standardized_rows, axis=0)
    normalized_gradient = layernorm_gradient * gain_float32
    input_gradient = inverse_deviation * (
        normalized_gradient
        - jnp.mean(normalized_gradient, axis=1, keepdims=True)
        - standardized_rows
        * jnp.mean(normalized_gradient * standardized_rows, axis=1, keepdims=True)
    )
    d_tokens = (up_rows.astype(jnp.float32) + input_gradient).astype(jnp.bfloat16)
    return (
        result.reshape(tokens.shape),
        d_tokens.reshape(tokens.shape),
        layernorm_output,
        context,
        d_qkv,
        up_rows,
        gain_products,
    )


def left_product(left, right):
    return lax.dot_general(
        left, right, (((0,), (0,)), ((), ())), preferred_element_type=jnp.float32
    )


def on_device(
    patches, visible_order, visible_counts, dest_rows, qkv_weight, out_weight, norm_gain, upstream
):
    qkv_cols = qkv_weight.shape[1]
    out_cols = out_weight.shape[1]
    gain_block = jnp.broadcast_to(norm_gain[:, None], (norm_gain.shape[0], 128))
    gathered = lax.all_gather(
        jnp.concatenate([qkv_weight, out_weight, gain_block], axis=1), "replica", axis=0, tiled=True
    )
    wqkv = gathered[:, :qkv_cols]
    wout = gathered[:, qkv_cols : qkv_cols + out_cols]
    gain = gathered[:, qkv_cols + out_cols]
    batches = lax.axis_size("batch")
    me_index = lax.axis_index("batch")
    cap = MEANVIS * batches
    width = wout.shape[1]
    slot = jnp.arange(MAXVIS, dtype=jnp.int32)
    sources = jnp.arange(batches, dtype=jnp.int32)
    counts_all = visible_counts[0].reshape(batches, batches)
    rows_all = dest_rows[0].reshape(batches, batches)
    mine = rows_all // cap == me_index
    src_count = jnp.sum(jnp.where(mine, counts_all, 0), axis=1)
    src_start = jnp.sum(jnp.where(mine, rows_all % cap, 0), axis=1)
    position = jnp.arange(cap, dtype=jnp.int32)
    hit = (position[:, None] >= src_start[None, :]) & (
        position[:, None] < (src_start + src_count)[None, :]
    )
    segment = jnp.sum(jnp.where(hit, sources[None, :], 0), axis=1)
    inside = jnp.sum(jnp.where(hit, position[:, None] - src_start[None, :], 0), axis=1)
    flat_rows = segment * MAXVIS + inside
    my_targets = jnp.take(rows_all, me_index, axis=0) // cap
    to_target = jnp.sum(
        jnp.where(my_targets[None, :] == sources[:, None], sources[None, :], 0), axis=1
    )
    my_counts = jnp.take(counts_all, me_index, axis=0)
    local_rows = jnp.take_along_axis(patches[0], visible_order[0, :, :MAXVIS, None], axis=1)
    live = slot[None, :] < src_count[:, None]
    pick = jnp.clip(src_start[:, None] + slot[None, :], 0, cap - 1)
    fetched = jnp.take(upstream[0], pick.reshape(-1), axis=0).reshape(batches, MAXVIS, width)
    backward_rows = jnp.where(live[..., None], fetched, jnp.zeros_like(fetched))
    returned = lax.all_to_all(backward_rows, "batch", split_axis=0, concat_axis=0, tiled=True)
    upward = jnp.take(returned, my_targets, axis=0)
    valid = slot[None, :] < my_counts[:, None]
    allowed = jnp.broadcast_to(valid[:, None, :], (batches, MAXVIS, MAXVIS))
    result, d_tokens, layernorm_output, context, d_qkv, up_rows, gain_products = layer_core(
        local_rows, upward, allowed, wqkv, wout, gain
    )
    came = lax.all_to_all(
        jnp.take(jnp.concatenate([result, d_tokens], axis=-1), to_target, axis=0),
        "batch",
        split_axis=0,
        concat_axis=0,
        tiled=True,
    )
    came_out = came[..., :width]
    came_grad = came[..., width:]
    layer_out = jnp.take(came_out.reshape(batches * MAXVIS, width), flat_rows, axis=0)
    d_packed = jnp.take(came_grad.reshape(batches * MAXVIS, width), flat_rows, axis=0)
    partial = jnp.concatenate(
        [
            left_product(layernorm_output, d_qkv).astype(jnp.bfloat16),
            left_product(context, up_rows).astype(jnp.bfloat16),
            jnp.broadcast_to(gain_products.astype(jnp.bfloat16)[:, None], (width, 128)),
        ],
        axis=1,
    )
    summed = lax.psum_scatter(partial, "replica", scatter_dimension=0, tiled=True)
    pieces = lax.all_to_all(
        summed.reshape(batches, -1, summed.shape[1]), "batch", split_axis=0, concat_axis=0, tiled=True
    )
    reduced = jnp.sum(pieces.astype(jnp.float32), axis=0).astype(jnp.bfloat16)
    summed = lax.all_to_all(
        jnp.broadcast_to(reduced[None], (batches,) + reduced.shape),
        "batch",
        split_axis=0,
        concat_axis=0,
        tiled=True,
    )
    summed = summed.reshape(-1, summed.shape[2]).astype(jnp.float32)
    grad_q = summed[:, :qkv_cols]
    grad_o = summed[:, qkv_cols : qkv_cols + out_cols]
    grad_g = summed[:, qkv_cols + out_cols]
    return (layer_out[None], d_packed[None], grad_q, grad_o, grad_g)


def solution(mesh):
    placed = (
        P("replica", "batch", None, None),
        P("replica", "batch", None),
        P("replica", None),
        P("replica", None),
        P("replica", None),
        P("replica", None),
        P("replica"),
        P("replica", "batch", None),
    )
    return jax.shard_map(
        on_device,
        mesh=mesh,
        in_specs=placed,
        out_specs=(
            P("replica", "batch", None),
            P("replica", "batch", None),
            P("replica", None),
            P("replica", None),
            P("replica"),
        ),
        check_vma=False,
    )
```

```python
import jax
import jax.numpy as jnp
from jax import lax
from jax.sharding import PartitionSpec as P

HEADS = 16
MAXVIS = 32
MEANVIS = 16


EPS = 1e-06
NEG = -1e30


def layer_core(tokens, upward, allowed, wqkv, wout, gain):
    groups, length, width = tokens.shape
    rows = groups * length
    head_dim = width // HEADS
    scale = head_dim ** (-0.5)
    f32 = jnp.float32
    x32 = tokens.astype(jnp.float32).reshape(rows, width)
    row_average = jnp.mean(x32, axis=1, keepdims=True)
    centered_rows = x32 - row_average
    inverse_deviation = lax.rsqrt(
        jnp.mean(centered_rows * centered_rows, axis=1, keepdims=True) + EPS
    )
    standardized_rows = centered_rows * inverse_deviation
    gain_float32 = gain.astype(jnp.float32)
    layernorm_output = (standardized_rows * gain_float32).astype(jnp.bfloat16)
    w3 = wqkv.reshape(width, 3, HEADS, head_dim)
    qkv = jnp.einsum("rc,cjhd->jhrd", layernorm_output, w3, preferred_element_type=f32).astype(
        jnp.bfloat16
    )
    qkv = qkv.reshape(3, HEADS, groups, length, head_dim)
    query, keys, values = qkv[0], qkv[1], qkv[2]
    scores = jnp.einsum("hgqd,hgkd->hgqk", query, keys, preferred_element_type=f32) * scale
    scores = jnp.where(allowed[None], scores, NEG)
    top = jnp.max(scores, axis=-1, keepdims=True)
    expd = jnp.exp(scores - top)
    probs = expd / jnp.sum(expd, axis=-1, keepdims=True)
    weights = probs.astype(jnp.bfloat16)
    context = jnp.einsum("hgqk,hgkd->hgqd", weights, values, preferred_element_type=f32).astype(
        jnp.bfloat16
    )
    wout3 = wout.reshape(HEADS, head_dim, width)
    projected = jnp.einsum("hgqd,hde->gqe", context, wout3, preferred_element_type=f32)
    result = (x32 + projected.reshape(rows, width)).astype(jnp.bfloat16)
    up3 = upward.reshape(groups, length, width)
    d_context = jnp.einsum("gqe,hde->hgqd", up3, wout3, preferred_element_type=f32).astype(
        jnp.bfloat16
    )
    d_values = jnp.einsum(
        "hgqk,hgqd->hgkd", weights, d_context, preferred_element_type=f32
    ).astype(jnp.bfloat16)
    d_weights = jnp.einsum("hgqd,hgkd->hgqk", d_context, values, preferred_element_type=f32)
    d_scores = (
        probs * (d_weights - jnp.sum(d_weights * probs, axis=-1, keepdims=True)) * scale
    ).astype(jnp.bfloat16)
    d_query = jnp.einsum(
        "hgqk,hgkd->hgqd", d_scores, keys, preferred_element_type=f32
    ).astype(jnp.bfloat16)
    d_keys = jnp.einsum(
        "hgqk,hgqd->hgkd", d_scores, query, preferred_element_type=f32
    ).astype(jnp.bfloat16)
    d_qkv = jnp.stack([d_query, d_keys, d_values])
    layernorm_gradient = jnp.einsum(
        "jhgqd,cjhd->gqc", d_qkv, w3, preferred_element_type=f32
    ).reshape(rows, width)
    gain_products = jnp.sum(layernorm_gradient * standardized_rows, axis=0)
    normalized_gradient = layernorm_gradient * gain_float32
    input_gradient = inverse_deviation * (
        normalized_gradient
        - jnp.mean(normalized_gradient, axis=1, keepdims=True)
        - standardized_rows
        * jnp.mean(normalized_gradient * standardized_rows, axis=1, keepdims=True)
    )
    up_rows = upward.reshape(rows, width)
    d_tokens = (up_rows.astype(jnp.float32) + input_gradient).astype(jnp.bfloat16)
    grad_qkv_part = jnp.einsum(
        "gqc,jhgqd->cjhd",
        layernorm_output.reshape(groups, length, width),
        d_qkv,
        preferred_element_type=f32,
    ).reshape(width, 3 * width)
    grad_out_part = jnp.einsum(
        "hgqd,gqe->hde", context, up3, preferred_element_type=f32
    ).reshape(width, width)
    return (
        result.reshape(tokens.shape),
        d_tokens.reshape(tokens.shape),
        grad_qkv_part,
        grad_out_part,
        gain_products,
    )


def on_device(
    patches, visible_order, visible_counts, dest_rows, qkv_weight, out_weight, norm_gain, upstream
):
    qkv_cols = qkv_weight.shape[1]
    out_cols = out_weight.shape[1]
    gain_block = jnp.broadcast_to(norm_gain[:, None], (norm_gain.shape[0], 128))
    gathered = lax.all_gather(
        jnp.concatenate([qkv_weight, out_weight, gain_block], axis=1), "replica", axis=0, tiled=True
    )
    wqkv = gathered[:, :qkv_cols]
    wout = gathered[:, qkv_cols : qkv_cols + out_cols]
    gain = gathered[:, qkv_cols + out_cols]
    batches = lax.axis_size("batch")
    me_index = lax.axis_index("batch")
    cap = MEANVIS * batches
    width = wout.shape[1]
    slot = jnp.arange(MAXVIS, dtype=jnp.int32)
    sources = jnp.arange(batches, dtype=jnp.int32)
    counts_all = visible_counts[0].reshape(batches, batches)
    rows_all = dest_rows[0].reshape(batches, batches)
    mine = rows_all // cap == me_index
    src_count = jnp.sum(jnp.where(mine, counts_all, 0), axis=1)
    src_start = jnp.sum(jnp.where(mine, rows_all % cap, 0), axis=1)
    position = jnp.arange(cap, dtype=jnp.int32)
    hit = (position[:, None] >= src_start[None, :]) & (
        position[:, None] < (src_start + src_count)[None, :]
    )
    segment = jnp.sum(jnp.where(hit, sources[None, :], 0), axis=1)
    inside = jnp.sum(jnp.where(hit, position[:, None] - src_start[None, :], 0), axis=1)
    flat_rows = segment * MAXVIS + inside
    my_targets = jnp.take(rows_all, me_index, axis=0) // cap
    to_target = jnp.sum(
        jnp.where(my_targets[None, :] == sources[:, None], sources[None, :], 0), axis=1
    )
    my_counts = jnp.take(counts_all, me_index, axis=0)
    local_rows = jnp.take_along_axis(patches[0], visible_order[0, :, :MAXVIS, None], axis=1)
    live = slot[None, :] < src_count[:, None]
    pick = jnp.clip(src_start[:, None] + slot[None, :], 0, cap - 1)
    fetched = jnp.take(upstream[0], pick.reshape(-1), axis=0).reshape(batches, MAXVIS, width)
    backward_rows = jnp.where(live[..., None], fetched, jnp.zeros_like(fetched))
    returned = lax.all_to_all(backward_rows, "batch", split_axis=0, concat_axis=0, tiled=True)
    upward = jnp.take(returned, my_targets, axis=0)
    valid = slot[None, :] < my_counts[:, None]
    allowed = jnp.broadcast_to(valid[:, None, :], (batches, MAXVIS, MAXVIS))
    result, d_tokens, grad_qkv_part, grad_out_part, gain_products = layer_core(
        local_rows, upward, allowed, wqkv, wout, gain
    )
    came = lax.all_to_all(
        jnp.take(jnp.concatenate([result, d_tokens], axis=-1), to_target, axis=0),
        "batch",
        split_axis=0,
        concat_axis=0,
        tiled=True,
    )
    came_out = came[..., :width]
    came_grad = came[..., width:]
    layer_out = jnp.take(came_out.reshape(batches * MAXVIS, width), flat_rows, axis=0)
    d_packed = jnp.take(came_grad.reshape(batches * MAXVIS, width), flat_rows, axis=0)
    partial = jnp.concatenate(
        [
            grad_qkv_part.astype(jnp.bfloat16),
            grad_out_part.astype(jnp.bfloat16),
            jnp.broadcast_to(gain_products.astype(jnp.bfloat16)[:, None], (width, 128)),
        ],
        axis=1,
    )
    summed = lax.psum_scatter(partial, "replica", scatter_dimension=0, tiled=True)
    pieces = lax.all_to_all(
        summed.reshape(batches, -1, summed.shape[1]), "batch", split_axis=0, concat_axis=0, tiled=True
    )
    reduced = jnp.sum(pieces.astype(jnp.float32), axis=0).astype(jnp.bfloat16)
    summed = lax.all_to_all(
        jnp.broadcast_to(reduced[None], (batches,) + reduced.shape),
        "batch",
        split_axis=0,
        concat_axis=0,
        tiled=True,
    )
    summed = summed.reshape(-1, summed.shape[2]).astype(jnp.float32)
    grad_q = summed[:, :qkv_cols]
    grad_o = summed[:, qkv_cols : qkv_cols + out_cols]
    grad_g = summed[:, qkv_cols + out_cols]
    return (layer_out[None], d_packed[None], grad_q, grad_o, grad_g)


def solution(mesh):
    placed = (
        P("replica", "batch", None, None),
        P("replica", "batch", None),
        P("replica", None),
        P("replica", None),
        P("replica", None),
        P("replica", None),
        P("replica"),
        P("replica", "batch", None),
    )

    return jax.shard_map(
        on_device,
        mesh=mesh,
        in_specs=placed,
        out_specs=(
            P("replica", "batch", None),
            P("replica", "batch", None),
            P("replica", None),
            P("replica", None),
            P("replica"),
        ),
        check_vma=False,
    )
```

```python
import jax
import jax.numpy as jnp
from jax import lax
from jax.sharding import PartitionSpec as P

HEADS = 16
MAXVIS = 32
MEANVIS = 16


EPS = 1e-06
NEG = -1e30


def layer_core(tokens, upward, allowed, wqkv, wout, gain):
    groups, length, width = tokens.shape
    rows = groups * length
    head_dim = width // HEADS
    scale = head_dim ** (-0.5)
    f32 = jnp.float32
    x32 = tokens.astype(jnp.float32).reshape(rows, width)
    row_average = jnp.mean(x32, axis=1, keepdims=True)
    centered_rows = x32 - row_average
    inverse_deviation = lax.rsqrt(
        jnp.mean(centered_rows * centered_rows, axis=1, keepdims=True) + EPS
    )
    standardized_rows = centered_rows * inverse_deviation
    gain_float32 = gain.astype(jnp.float32)
    layernorm_output = (standardized_rows * gain_float32).astype(jnp.bfloat16)
    qkv = jnp.dot(layernorm_output, wqkv, preferred_element_type=f32).astype(jnp.bfloat16)
    qkv = jnp.transpose(qkv.reshape(groups, length, 3, HEADS, head_dim), (2, 3, 0, 1, 4))
    query, keys, values = qkv[0], qkv[1], qkv[2]
    scores = jnp.einsum("hgqd,hgkd->hgqk", query, keys, preferred_element_type=f32) * scale
    scores = jnp.where(allowed[None], scores, NEG)
    top = jnp.max(scores, axis=-1, keepdims=True)
    expd = jnp.exp(scores - top)
    probs = expd / jnp.sum(expd, axis=-1, keepdims=True)
    weights = probs.astype(jnp.bfloat16)
    context = jnp.einsum("hgqk,hgkd->hgqd", weights, values, preferred_element_type=f32).astype(
        jnp.bfloat16
    )
    wout3 = wout.reshape(HEADS, head_dim, width)
    projected = jnp.einsum("hgqd,hde->gqe", context, wout3, preferred_element_type=f32)
    result = (x32 + projected.reshape(rows, width)).astype(jnp.bfloat16)
    up3 = upward.reshape(groups, length, width)
    d_context = jnp.einsum("gqe,hde->hgqd", up3, wout3, preferred_element_type=f32).astype(
        jnp.bfloat16
    )
    d_values = jnp.einsum(
        "hgqk,hgqd->hgkd", weights, d_context, preferred_element_type=f32
    ).astype(jnp.bfloat16)
    d_weights = jnp.einsum("hgqd,hgkd->hgqk", d_context, values, preferred_element_type=f32)
    d_scores = (
        probs * (d_weights - jnp.sum(d_weights * probs, axis=-1, keepdims=True)) * scale
    ).astype(jnp.bfloat16)
    d_query = jnp.einsum(
        "hgqk,hgkd->hgqd", d_scores, keys, preferred_element_type=f32
    ).astype(jnp.bfloat16)
    d_keys = jnp.einsum(
        "hgqk,hgqd->hgkd", d_scores, query, preferred_element_type=f32
    ).astype(jnp.bfloat16)
    d_qkv = jnp.transpose(jnp.stack([d_query, d_keys, d_values]), (2, 3, 0, 1, 4)).reshape(
        rows, 3 * width
    )
    layernorm_gradient = lax.dot_general(
        d_qkv, wqkv, (((1,), (1,)), ((), ())), preferred_element_type=f32
    )
    gain_products = jnp.sum(layernorm_gradient * standardized_rows, axis=0)
    normalized_gradient = layernorm_gradient * gain_float32
    input_gradient = inverse_deviation * (
        normalized_gradient
        - jnp.mean(normalized_gradient, axis=1, keepdims=True)
        - standardized_rows
        * jnp.mean(normalized_gradient * standardized_rows, axis=1, keepdims=True)
    )
    up_rows = upward.reshape(rows, width)
    d_tokens = (up_rows.astype(jnp.float32) + input_gradient).astype(jnp.bfloat16)
    grad_qkv_part = left_product(layernorm_output, d_qkv)
    grad_out_part = jnp.einsum(
        "hgqd,gqe->hde", context, up3, preferred_element_type=f32
    ).reshape(width, width)
    return (
        result.reshape(tokens.shape),
        d_tokens.reshape(tokens.shape),
        grad_qkv_part,
        grad_out_part,
        gain_products,
    )


def left_product(left, right):
    return lax.dot_general(
        left, right, (((0,), (0,)), ((), ())), preferred_element_type=jnp.float32
    )


def on_device(
    patches, visible_order, visible_counts, dest_rows, qkv_weight, out_weight, norm_gain, upstream
):
    qkv_cols = qkv_weight.shape[1]
    out_cols = out_weight.shape[1]
    gain_block = jnp.broadcast_to(norm_gain[:, None], (norm_gain.shape[0], 128))
    gathered = lax.all_gather(
        jnp.concatenate([qkv_weight, out_weight, gain_block], axis=1), "replica", axis=0, tiled=True
    )
    wqkv = gathered[:, :qkv_cols]
    wout = gathered[:, qkv_cols : qkv_cols + out_cols]
    gain = gathered[:, qkv_cols + out_cols]
    batches = lax.axis_size("batch")
    me_index = lax.axis_index("batch")
    cap = MEANVIS * batches
    width = wout.shape[1]
    slot = jnp.arange(MAXVIS, dtype=jnp.int32)
    sources = jnp.arange(batches, dtype=jnp.int32)
    counts_all = visible_counts[0].reshape(batches, batches)
    rows_all = dest_rows[0].reshape(batches, batches)
    mine = rows_all // cap == me_index
    src_count = jnp.sum(jnp.where(mine, counts_all, 0), axis=1)
    src_start = jnp.sum(jnp.where(mine, rows_all % cap, 0), axis=1)
    position = jnp.arange(cap, dtype=jnp.int32)
    hit = (position[:, None] >= src_start[None, :]) & (
        position[:, None] < (src_start + src_count)[None, :]
    )
    segment = jnp.sum(jnp.where(hit, sources[None, :], 0), axis=1)
    inside = jnp.sum(jnp.where(hit, position[:, None] - src_start[None, :], 0), axis=1)
    flat_rows = segment * MAXVIS + inside
    my_targets = jnp.take(rows_all, me_index, axis=0) // cap
    to_target = jnp.sum(
        jnp.where(my_targets[None, :] == sources[:, None], sources[None, :], 0), axis=1
    )
    my_counts = jnp.take(counts_all, me_index, axis=0)
    local_rows = jnp.take_along_axis(patches[0], visible_order[0, :, :MAXVIS, None], axis=1)
    live = slot[None, :] < src_count[:, None]
    pick = jnp.clip(src_start[:, None] + slot[None, :], 0, cap - 1)
    fetched = jnp.take(upstream[0], pick.reshape(-1), axis=0).reshape(batches, MAXVIS, width)
    backward_rows = jnp.where(live[..., None], fetched, jnp.zeros_like(fetched))
    returned = lax.all_to_all(backward_rows, "batch", split_axis=0, concat_axis=0, tiled=True)
    upward = jnp.take(returned, my_targets, axis=0)
    valid = slot[None, :] < my_counts[:, None]
    allowed = jnp.broadcast_to(valid[:, None, :], (batches, MAXVIS, MAXVIS))
    result, d_tokens, grad_qkv_part, grad_out_part, gain_products = layer_core(
        local_rows, upward, allowed, wqkv, wout, gain
    )
    came = lax.all_to_all(
        jnp.take(jnp.concatenate([result, d_tokens], axis=-1), to_target, axis=0),
        "batch",
        split_axis=0,
        concat_axis=0,
        tiled=True,
    )
    came_out = came[..., :width]
    came_grad = came[..., width:]
    layer_out = jnp.take(came_out.reshape(batches * MAXVIS, width), flat_rows, axis=0)
    d_packed = jnp.take(came_grad.reshape(batches * MAXVIS, width), flat_rows, axis=0)
    partial = jnp.concatenate(
        [
            grad_qkv_part.astype(jnp.bfloat16),
            grad_out_part.astype(jnp.bfloat16),
            jnp.broadcast_to(gain_products.astype(jnp.bfloat16)[:, None], (width, 128)),
        ],
        axis=1,
    )
    summed = lax.psum_scatter(partial, "replica", scatter_dimension=0, tiled=True)
    pieces = lax.all_to_all(
        summed.reshape(batches, -1, summed.shape[1]), "batch", split_axis=0, concat_axis=0, tiled=True
    )
    reduced = jnp.sum(pieces.astype(jnp.float32), axis=0).astype(jnp.bfloat16)
    summed = lax.all_to_all(
        jnp.broadcast_to(reduced[None], (batches,) + reduced.shape),
        "batch",
        split_axis=0,
        concat_axis=0,
        tiled=True,
    )
    summed = summed.reshape(-1, summed.shape[2]).astype(jnp.float32)
    grad_q = summed[:, :qkv_cols]
    grad_o = summed[:, qkv_cols : qkv_cols + out_cols]
    grad_g = summed[:, qkv_cols + out_cols]
    return (layer_out[None], d_packed[None], grad_q, grad_o, grad_g)


def solution(mesh):
    placed = (
        P("replica", "batch", None, None),
        P("replica", "batch", None),
        P("replica", None),
        P("replica", None),
        P("replica", None),
        P("replica", None),
        P("replica"),
        P("replica", "batch", None),
    )

    return jax.shard_map(
        on_device,
        mesh=mesh,
        in_specs=placed,
        out_specs=(
            P("replica", "batch", None),
            P("replica", "batch", None),
            P("replica", None),
            P("replica", None),
            P("replica"),
        ),
        check_vma=False,
    )
```

```python
import jax
import jax.numpy as jnp
from jax import lax
from jax.sharding import PartitionSpec as P

HEADS = 16
MAXVIS = 32
MEANVIS = 16


EPS = 1e-06
NEG = -1e30


def layer_core(tokens, upward, allowed, wqkv, wout, gain):
    groups, length, width = tokens.shape
    rows = groups * length
    head_dim = width // HEADS
    scale = head_dim ** (-0.5)
    f32 = jnp.float32
    x32 = tokens.astype(jnp.float32).reshape(rows, width)
    row_average = jnp.mean(x32, axis=1, keepdims=True)
    centered_rows = x32 - row_average
    inverse_deviation = lax.rsqrt(
        jnp.mean(centered_rows * centered_rows, axis=1, keepdims=True) + EPS
    )
    standardized_rows = centered_rows * inverse_deviation
    gain_float32 = gain.astype(jnp.float32)
    layernorm_output = (standardized_rows * gain_float32).astype(jnp.bfloat16)
    qkv = jnp.dot(layernorm_output, wqkv, preferred_element_type=f32).astype(jnp.bfloat16)
    qkv = jnp.transpose(qkv.reshape(groups, length, 3, HEADS, head_dim), (2, 3, 0, 1, 4))
    query, keys, values = qkv[0], qkv[1], qkv[2]
    scores = jnp.einsum("hgqd,hgkd->hgqk", query, keys, preferred_element_type=f32) * scale
    scores = jnp.where(allowed[None], scores, NEG)
    top = jnp.max(scores, axis=-1, keepdims=True)
    expd = jnp.exp(scores - top)
    probs = expd / jnp.sum(expd, axis=-1, keepdims=True)
    weights = probs.astype(jnp.bfloat16)
    context = jnp.einsum("hgqk,hgkd->hgqd", weights, values, preferred_element_type=f32).astype(
        jnp.bfloat16
    )
    wout3 = wout.reshape(HEADS, head_dim, width)
    projected = jnp.einsum("hgqd,hde->gqe", context, wout3, preferred_element_type=f32)
    result = (x32 + projected.reshape(rows, width)).astype(jnp.bfloat16)
    up3 = upward.reshape(groups, length, width)
    d_context = jnp.einsum("gqe,hde->hgqd", up3, wout3, preferred_element_type=f32).astype(
        jnp.bfloat16
    )
    d_values = jnp.einsum(
        "hgqk,hgqd->hgkd", weights, d_context, preferred_element_type=f32
    ).astype(jnp.bfloat16)
    d_weights = jnp.einsum("hgqd,hgkd->hgqk", d_context, values, preferred_element_type=f32)
    d_scores = (
        probs * (d_weights - jnp.sum(d_weights * probs, axis=-1, keepdims=True)) * scale
    ).astype(jnp.bfloat16)
    d_query = jnp.einsum(
        "hgqk,hgkd->hgqd", d_scores, keys, preferred_element_type=f32
    ).astype(jnp.bfloat16)
    d_keys = jnp.einsum(
        "hgqk,hgqd->hgkd", d_scores, query, preferred_element_type=f32
    ).astype(jnp.bfloat16)
    d_qkv = jnp.transpose(jnp.stack([d_query, d_keys, d_values]), (2, 3, 0, 1, 4)).reshape(
        rows, 3 * width
    )
    layernorm_gradient = lax.dot_general(
        d_qkv, wqkv, (((1,), (1,)), ((), ())), preferred_element_type=f32
    )
    gain_products = jnp.sum(layernorm_gradient * standardized_rows, axis=0)
    normalized_gradient = layernorm_gradient * gain_float32
    input_gradient = inverse_deviation * (
        normalized_gradient
        - jnp.mean(normalized_gradient, axis=1, keepdims=True)
        - standardized_rows
        * jnp.mean(normalized_gradient * standardized_rows, axis=1, keepdims=True)
    )
    up_rows = upward.reshape(rows, width)
    d_tokens = (up_rows.astype(jnp.float32) + input_gradient).astype(jnp.bfloat16)
    grad_qkv_part = left_product(layernorm_output, d_qkv)
    grad_out_part = jnp.einsum(
        "hgqd,gqe->hde", context, up3, preferred_element_type=f32
    ).reshape(width, width)
    return (
        result.reshape(tokens.shape),
        d_tokens.reshape(tokens.shape),
        grad_qkv_part,
        grad_out_part,
        gain_products,
    )


def left_product(left, right):
    return lax.dot_general(
        left, right, (((0,), (0,)), ((), ())), preferred_element_type=jnp.float32
    )


def on_device(
    patches, visible_order, visible_counts, dest_rows, qkv_weight, out_weight, norm_gain, upstream
):
    qkv_cols = qkv_weight.shape[1]
    out_cols = out_weight.shape[1]
    gain_block = jnp.broadcast_to(norm_gain[:, None], (norm_gain.shape[0], 128))
    gathered = lax.all_gather(
        jnp.concatenate([qkv_weight, out_weight, gain_block], axis=1), "replica", axis=0, tiled=True
    )
    wqkv = gathered[:, :qkv_cols]
    wout = gathered[:, qkv_cols : qkv_cols + out_cols]
    gain = gathered[:, qkv_cols + out_cols]
    batches = lax.axis_size("batch")
    me_index = lax.axis_index("batch")
    cap = MEANVIS * batches
    width = wout.shape[1]
    slot = jnp.arange(MAXVIS, dtype=jnp.int32)
    sources = jnp.arange(batches, dtype=jnp.int32)
    counts_all = visible_counts[0].reshape(batches, batches)
    rows_all = dest_rows[0].reshape(batches, batches)
    mine = rows_all // cap == me_index
    src_count = jnp.sum(jnp.where(mine, counts_all, 0), axis=1)
    src_start = jnp.sum(jnp.where(mine, rows_all % cap, 0), axis=1)
    position = jnp.arange(cap, dtype=jnp.int32)
    hit = (position[:, None] >= src_start[None, :]) & (
        position[:, None] < (src_start + src_count)[None, :]
    )
    segment = jnp.sum(jnp.where(hit, sources[None, :], 0), axis=1)
    inside = jnp.sum(jnp.where(hit, position[:, None] - src_start[None, :], 0), axis=1)
    flat_rows = segment * MAXVIS + inside
    my_targets = jnp.take(rows_all, me_index, axis=0) // cap
    to_target = jnp.sum(
        jnp.where(my_targets[None, :] == sources[:, None], sources[None, :], 0), axis=1
    )
    my_counts = jnp.take(counts_all, me_index, axis=0)
    local_rows = jnp.take_along_axis(patches[0], visible_order[0, :, :MAXVIS, None], axis=1)
    live = slot[None, :] < src_count[:, None]
    pick = jnp.clip(src_start[:, None] + slot[None, :], 0, cap - 1)
    fetched = jnp.take(upstream[0], pick.reshape(-1), axis=0).reshape(batches, MAXVIS, width)
    backward_rows = jnp.where(live[..., None], fetched, jnp.zeros_like(fetched))
    returned = lax.all_to_all(backward_rows, "batch", split_axis=0, concat_axis=0, tiled=True)
    upward = jnp.take(returned, my_targets, axis=0)
    valid = slot[None, :] < my_counts[:, None]
    allowed = jnp.broadcast_to(valid[:, None, :], (batches, MAXVIS, MAXVIS))
    result, d_tokens, grad_qkv_part, grad_out_part, gain_products = layer_core(
        local_rows, upward, allowed, wqkv, wout, gain
    )
    came = lax.all_to_all(
        jnp.take(jnp.concatenate([result, d_tokens], axis=-1), to_target, axis=0),
        "batch",
        split_axis=0,
        concat_axis=0,
        tiled=True,
    )
    came_out = came[..., :width]
    came_grad = came[..., width:]
    layer_out = jnp.take(came_out.reshape(batches * MAXVIS, width), flat_rows, axis=0)
    d_packed = jnp.take(came_grad.reshape(batches * MAXVIS, width), flat_rows, axis=0)
    side = jnp.concatenate(
        [
            grad_out_part.astype(jnp.bfloat16),
            jnp.broadcast_to(gain_products.astype(jnp.bfloat16)[:, None], (width, 128)),
        ],
        axis=1,
    )
    replicas = lax.axis_size("replica")
    side = lax.all_to_all(
        side.reshape(replicas, -1, side.shape[1]), "replica", split_axis=0, concat_axis=0, tiled=True
    )
    side = jnp.sum(side.astype(jnp.float32), axis=0).astype(jnp.bfloat16)
    summed = lax.psum_scatter(
        grad_qkv_part.astype(jnp.bfloat16), "replica", scatter_dimension=0, tiled=True
    )
    summed = jnp.concatenate([summed, side], axis=1)
    pieces = lax.all_to_all(
        summed.reshape(batches, -1, summed.shape[1]), "batch", split_axis=0, concat_axis=0, tiled=True
    )
    reduced = jnp.sum(pieces.astype(jnp.float32), axis=0).astype(jnp.bfloat16)
    summed = lax.all_to_all(
        jnp.broadcast_to(reduced[None], (batches,) + reduced.shape),
        "batch",
        split_axis=0,
        concat_axis=0,
        tiled=True,
    )
    summed = summed.reshape(-1, summed.shape[2]).astype(jnp.float32)
    grad_q = summed[:, :qkv_cols]
    grad_o = summed[:, qkv_cols : qkv_cols + out_cols]
    grad_g = summed[:, qkv_cols + out_cols]
    return (layer_out[None], d_packed[None], grad_q, grad_o, grad_g)


def solution(mesh):
    placed = (
        P("replica", "batch", None, None),
        P("replica", "batch", None),
        P("replica", None),
        P("replica", None),
        P("replica", None),
        P("replica", None),
        P("replica"),
        P("replica", "batch", None),
    )

    return jax.shard_map(
        on_device,
        mesh=mesh,
        in_specs=placed,
        out_specs=(
            P("replica", "batch", None),
            P("replica", "batch", None),
            P("replica", None),
            P("replica", None),
            P("replica"),
        ),
        check_vma=False,
    )
```

```python
import jax
import jax.numpy as jnp
from jax import lax
from jax.sharding import PartitionSpec as P

HEADS = 16
MAXVIS = 32
MEANVIS = 16


EPS = 1e-06
NEG = -1e30


def layer_core(tokens, upward, allowed, wqkv, wout, gain):
    groups, length, width = tokens.shape
    rows = groups * length
    head_dim = width // HEADS
    scale = head_dim ** (-0.5)
    f32 = jnp.float32
    x32 = tokens.astype(jnp.float32).reshape(rows, width)
    row_average = jnp.mean(x32, axis=1, keepdims=True)
    centered_rows = x32 - row_average
    inverse_deviation = lax.rsqrt(
        jnp.mean(centered_rows * centered_rows, axis=1, keepdims=True) + EPS
    )
    standardized_rows = centered_rows * inverse_deviation
    gain_float32 = gain.astype(jnp.float32)
    layernorm_output = (standardized_rows * gain_float32).astype(jnp.bfloat16)
    qkv = jnp.dot(layernorm_output, wqkv, preferred_element_type=f32).astype(jnp.bfloat16)
    qkv = jnp.transpose(qkv.reshape(groups, length, 3, HEADS, head_dim), (2, 3, 0, 1, 4))
    query, keys, values = qkv[0], qkv[1], qkv[2]
    scores = jnp.einsum("hgqd,hgkd->hgqk", query, keys, preferred_element_type=f32) * scale
    scores = jnp.where(allowed[None], scores, NEG)
    top = jnp.max(scores, axis=-1, keepdims=True)
    expd = jnp.exp(scores - top)
    probs = expd / jnp.sum(expd, axis=-1, keepdims=True)
    weights = probs.astype(jnp.bfloat16)
    context = jnp.einsum("hgqk,hgkd->hgqd", weights, values, preferred_element_type=f32).astype(
        jnp.bfloat16
    )
    wout3 = wout.reshape(HEADS, head_dim, width)
    projected = jnp.einsum("hgqd,hde->gqe", context, wout3, preferred_element_type=f32)
    result = (x32 + projected.reshape(rows, width)).astype(jnp.bfloat16)
    up3 = upward.reshape(groups, length, width)
    d_context = jnp.einsum("gqe,hde->hgqd", up3, wout3, preferred_element_type=f32).astype(
        jnp.bfloat16
    )
    d_values = jnp.einsum(
        "hgqk,hgqd->hgkd", weights, d_context, preferred_element_type=f32
    ).astype(jnp.bfloat16)
    d_weights = jnp.einsum("hgqd,hgkd->hgqk", d_context, values, preferred_element_type=f32)
    d_scores = (
        probs * (d_weights - jnp.sum(d_weights * probs, axis=-1, keepdims=True)) * scale
    ).astype(jnp.bfloat16)
    d_query = jnp.einsum(
        "hgqk,hgkd->hgqd", d_scores, keys, preferred_element_type=f32
    ).astype(jnp.bfloat16)
    d_keys = jnp.einsum(
        "hgqk,hgqd->hgkd", d_scores, query, preferred_element_type=f32
    ).astype(jnp.bfloat16)
    d_qkv = jnp.transpose(jnp.stack([d_query, d_keys, d_values]), (2, 3, 0, 1, 4)).reshape(
        rows, 3 * width
    )
    layernorm_gradient = lax.dot_general(
        d_qkv, wqkv, (((1,), (1,)), ((), ())), preferred_element_type=f32
    )
    gain_products = jnp.sum(layernorm_gradient * standardized_rows, axis=0)
    normalized_gradient = layernorm_gradient * gain_float32
    input_gradient = inverse_deviation * (
        normalized_gradient
        - jnp.mean(normalized_gradient, axis=1, keepdims=True)
        - standardized_rows
        * jnp.mean(normalized_gradient * standardized_rows, axis=1, keepdims=True)
    )
    up_rows = upward.reshape(rows, width)
    d_tokens = (up_rows.astype(jnp.float32) + input_gradient).astype(jnp.bfloat16)
    grad_qkv_part = left_product(layernorm_output, d_qkv)
    grad_out_part = jnp.einsum(
        "hgqd,gqe->hde", context, up3, preferred_element_type=f32
    ).reshape(width, width)
    return (
        result.reshape(tokens.shape),
        d_tokens.reshape(tokens.shape),
        grad_qkv_part,
        grad_out_part,
        gain_products,
    )


def left_product(left, right):
    return lax.dot_general(
        left, right, (((0,), (0,)), ((), ())), preferred_element_type=jnp.float32
    )


def on_device(
    patches, visible_order, visible_counts, dest_rows, qkv_weight, out_weight, norm_gain, upstream
):
    qkv_cols = qkv_weight.shape[1]
    out_cols = out_weight.shape[1]
    gain_block = jnp.broadcast_to(norm_gain[:, None], (norm_gain.shape[0], 128))
    gathered = lax.all_gather(
        jnp.concatenate([qkv_weight, out_weight, gain_block], axis=1), "replica", axis=0, tiled=True
    )
    wqkv = gathered[:, :qkv_cols]
    wout = gathered[:, qkv_cols : qkv_cols + out_cols]
    gain = gathered[:, qkv_cols + out_cols]
    batches = lax.axis_size("batch")
    me_index = lax.axis_index("batch")
    cap = MEANVIS * batches
    width = wout.shape[1]
    slot = jnp.arange(MAXVIS, dtype=jnp.int32)
    sources = jnp.arange(batches, dtype=jnp.int32)
    counts_all = visible_counts[0].reshape(batches, batches)
    rows_all = dest_rows[0].reshape(batches, batches)
    mine = rows_all // cap == me_index
    src_count = jnp.sum(jnp.where(mine, counts_all, 0), axis=1)
    src_start = jnp.sum(jnp.where(mine, rows_all % cap, 0), axis=1)
    position = jnp.arange(cap, dtype=jnp.int32)
    hit = (position[:, None] >= src_start[None, :]) & (
        position[:, None] < (src_start + src_count)[None, :]
    )
    segment = jnp.sum(jnp.where(hit, sources[None, :], 0), axis=1)
    inside = jnp.sum(jnp.where(hit, position[:, None] - src_start[None, :], 0), axis=1)
    flat_rows = segment * MAXVIS + inside
    my_targets = jnp.take(rows_all, me_index, axis=0) // cap
    to_target = jnp.sum(
        jnp.where(my_targets[None, :] == sources[:, None], sources[None, :], 0), axis=1
    )
    my_counts = jnp.take(counts_all, me_index, axis=0)
    local_rows = jnp.take_along_axis(patches[0], visible_order[0, :, :MAXVIS, None], axis=1)
    live = slot[None, :] < src_count[:, None]
    pick = jnp.clip(src_start[:, None] + slot[None, :], 0, cap - 1)
    fetched = jnp.take(upstream[0], pick.reshape(-1), axis=0).reshape(batches, MAXVIS, width)
    backward_rows = jnp.where(live[..., None], fetched, jnp.zeros_like(fetched))
    returned = lax.all_to_all(backward_rows, "batch", split_axis=0, concat_axis=0, tiled=True)
    upward = jnp.take(returned, my_targets, axis=0)
    valid = slot[None, :] < my_counts[:, None]
    allowed = jnp.broadcast_to(valid[:, None, :], (batches, MAXVIS, MAXVIS))
    result, d_tokens, grad_qkv_part, grad_out_part, gain_products = layer_core(
        local_rows, upward, allowed, wqkv, wout, gain
    )
    came = lax.all_to_all(
        jnp.take(jnp.concatenate([result, d_tokens], axis=-1), to_target, axis=0),
        "batch",
        split_axis=0,
        concat_axis=0,
        tiled=True,
    )
    came_out = came[..., :width]
    came_grad = came[..., width:]
    layer_out = jnp.take(came_out.reshape(batches * MAXVIS, width), flat_rows, axis=0)
    d_packed = jnp.take(came_grad.reshape(batches * MAXVIS, width), flat_rows, axis=0)
    partial = jnp.concatenate(
        [grad_qkv_part.astype(jnp.bfloat16), grad_out_part.astype(jnp.bfloat16)], axis=1
    )
    summed = lax.psum_scatter(partial, "replica", scatter_dimension=0, tiled=True)
    replicas = lax.axis_size("replica")
    gain_sum = lax.all_to_all(
        gain_products.astype(jnp.bfloat16).reshape(replicas, -1),
        "replica",
        split_axis=0,
        concat_axis=0,
        tiled=True,
    )
    gain_sum = jnp.sum(gain_sum.astype(jnp.float32), axis=0).astype(jnp.bfloat16)
    summed = jnp.concatenate(
        [summed, jnp.broadcast_to(gain_sum[:, None], (gain_sum.shape[0], 128))], axis=1
    )
    pieces = lax.all_to_all(
        summed.reshape(batches, -1, summed.shape[1]), "batch", split_axis=0, concat_axis=0, tiled=True
    )
    reduced = jnp.sum(pieces.astype(jnp.float32), axis=0).astype(jnp.bfloat16)
    summed = lax.all_to_all(
        jnp.broadcast_to(reduced[None], (batches,) + reduced.shape),
        "batch",
        split_axis=0,
        concat_axis=0,
        tiled=True,
    )
    summed = summed.reshape(-1, summed.shape[2]).astype(jnp.float32)
    grad_q = summed[:, :qkv_cols]
    grad_o = summed[:, qkv_cols : qkv_cols + out_cols]
    grad_g = summed[:, qkv_cols + out_cols]
    return (layer_out[None], d_packed[None], grad_q, grad_o, grad_g)


def solution(mesh):
    placed = (
        P("replica", "batch", None, None),
        P("replica", "batch", None),
        P("replica", None),
        P("replica", None),
        P("replica", None),
        P("replica", None),
        P("replica"),
        P("replica", "batch", None),
    )

    return jax.shard_map(
        on_device,
        mesh=mesh,
        in_specs=placed,
        out_specs=(
            P("replica", "batch", None),
            P("replica", "batch", None),
            P("replica", None),
            P("replica", None),
            P("replica"),
        ),
        check_vma=False,
    )
```

```python
import jax
import jax.numpy as jnp
from jax import lax
from jax.sharding import PartitionSpec as P

HEADS = 16
MAXVIS = 32
MEANVIS = 16


EPS = 1e-06
NEG = -1e30


def layer_core(tokens, upward, allowed, wqkv, wout, gain):
    groups, length, width = tokens.shape
    rows = groups * length
    head_dim = width // HEADS
    scale = head_dim ** (-0.5)
    f32 = jnp.float32
    x32 = tokens.astype(jnp.float32).reshape(rows, width)
    row_average = jnp.mean(x32, axis=1, keepdims=True)
    centered_rows = x32 - row_average
    inverse_deviation = lax.rsqrt(
        jnp.mean(centered_rows * centered_rows, axis=1, keepdims=True) + EPS
    )
    standardized_rows = centered_rows * inverse_deviation
    gain_float32 = gain.astype(jnp.float32)
    layernorm_output = (standardized_rows * gain_float32).astype(jnp.bfloat16)
    qkv = jnp.dot(layernorm_output, wqkv, preferred_element_type=f32).astype(jnp.bfloat16)
    qkv = jnp.transpose(qkv.reshape(groups, length, 3, HEADS, head_dim), (2, 3, 0, 1, 4))
    query, keys, values = qkv[0], qkv[1], qkv[2]
    scores = jnp.einsum("hgqd,hgkd->hgqk", query, keys, preferred_element_type=f32) * scale
    scores = jnp.where(allowed[None], scores, NEG)
    top = jnp.max(scores, axis=-1, keepdims=True)
    expd = jnp.exp(scores - top)
    probs = expd / jnp.sum(expd, axis=-1, keepdims=True)
    weights = probs.astype(jnp.bfloat16)
    context = jnp.einsum("hgqk,hgkd->hgqd", weights, values, preferred_element_type=f32).astype(
        jnp.bfloat16
    )
    context_rows = jnp.transpose(context, (1, 2, 0, 3)).reshape(rows, width)
    result = (x32 + jnp.dot(context_rows, wout, preferred_element_type=f32)).astype(jnp.bfloat16)
    up_rows = upward.reshape(rows, width)
    d_context = lax.dot_general(
        up_rows, wout, (((1,), (1,)), ((), ())), preferred_element_type=f32
    ).astype(jnp.bfloat16)
    d_context = jnp.transpose(d_context.reshape(groups, length, HEADS, head_dim), (2, 0, 1, 3))
    d_values = jnp.einsum(
        "hgqk,hgqd->hgkd", weights, d_context, preferred_element_type=f32
    ).astype(jnp.bfloat16)
    d_weights = jnp.einsum("hgqd,hgkd->hgqk", d_context, values, preferred_element_type=f32)
    d_scores = (
        probs * (d_weights - jnp.sum(d_weights * probs, axis=-1, keepdims=True)) * scale
    ).astype(jnp.bfloat16)
    d_query = jnp.einsum(
        "hgqk,hgkd->hgqd", d_scores, keys, preferred_element_type=f32
    ).astype(jnp.bfloat16)
    d_keys = jnp.einsum(
        "hgqk,hgqd->hgkd", d_scores, query, preferred_element_type=f32
    ).astype(jnp.bfloat16)
    d_qkv = jnp.transpose(jnp.stack([d_query, d_keys, d_values]), (2, 3, 0, 1, 4)).reshape(
        rows, 3 * width
    )
    layernorm_gradient = lax.dot_general(
        d_qkv, wqkv, (((1,), (1,)), ((), ())), preferred_element_type=f32
    )
    gain_products = jnp.sum(layernorm_gradient * standardized_rows, axis=0)
    normalized_gradient = layernorm_gradient * gain_float32
    input_gradient = inverse_deviation * (
        normalized_gradient
        - jnp.mean(normalized_gradient, axis=1, keepdims=True)
        - standardized_rows
        * jnp.mean(normalized_gradient * standardized_rows, axis=1, keepdims=True)
    )
    d_tokens = (up_rows.astype(jnp.float32) + input_gradient).astype(jnp.bfloat16)
    grad_qkv_part = left_product(layernorm_output, d_qkv)
    grad_out_part = left_product(context_rows, up_rows)
    return (
        result.reshape(tokens.shape),
        d_tokens.reshape(tokens.shape),
        grad_qkv_part,
        grad_out_part,
        gain_products,
    )


def left_product(left, right):
    return lax.dot_general(
        left, right, (((0,), (0,)), ((), ())), preferred_element_type=jnp.float32
    )


def on_device(
    patches, visible_order, visible_counts, dest_rows, qkv_weight, out_weight, norm_gain, upstream
):
    qkv_cols = qkv_weight.shape[1]
    out_cols = out_weight.shape[1]
    gain_block = jnp.broadcast_to(norm_gain[:, None], (norm_gain.shape[0], 128))
    gathered = lax.all_gather(
        jnp.concatenate([qkv_weight, out_weight, gain_block], axis=1), "replica", axis=0, tiled=True
    )
    wqkv = gathered[:, :qkv_cols]
    wout = gathered[:, qkv_cols : qkv_cols + out_cols]
    gain = gathered[:, qkv_cols + out_cols]
    batches = lax.axis_size("batch")
    me_index = lax.axis_index("batch")
    cap = MEANVIS * batches
    width = wout.shape[1]
    slot = jnp.arange(MAXVIS, dtype=jnp.int32)
    sources = jnp.arange(batches, dtype=jnp.int32)
    counts_all = visible_counts[0].reshape(batches, batches)
    rows_all = dest_rows[0].reshape(batches, batches)
    mine = rows_all // cap == me_index
    src_count = jnp.sum(jnp.where(mine, counts_all, 0), axis=1)
    src_start = jnp.sum(jnp.where(mine, rows_all % cap, 0), axis=1)
    position = jnp.arange(cap, dtype=jnp.int32)
    hit = (position[:, None] >= src_start[None, :]) & (
        position[:, None] < (src_start + src_count)[None, :]
    )
    segment = jnp.sum(jnp.where(hit, sources[None, :], 0), axis=1)
    inside = jnp.sum(jnp.where(hit, position[:, None] - src_start[None, :], 0), axis=1)
    flat_rows = segment * MAXVIS + inside
    my_targets = jnp.take(rows_all, me_index, axis=0) // cap
    to_target = jnp.sum(
        jnp.where(my_targets[None, :] == sources[:, None], sources[None, :], 0), axis=1
    )
    my_counts = jnp.take(counts_all, me_index, axis=0)
    local_rows = jnp.take_along_axis(patches[0], visible_order[0, :, :MAXVIS, None], axis=1)
    live = slot[None, :] < src_count[:, None]
    pick = jnp.clip(src_start[:, None] + slot[None, :], 0, cap - 1)
    fetched = jnp.take(upstream[0], pick.reshape(-1), axis=0).reshape(batches, MAXVIS, width)
    backward_rows = jnp.where(live[..., None], fetched, jnp.zeros_like(fetched))
    returned = lax.all_to_all(backward_rows, "batch", split_axis=0, concat_axis=0, tiled=True)
    upward = jnp.take(returned, my_targets, axis=0)
    valid = slot[None, :] < my_counts[:, None]
    allowed = jnp.broadcast_to(valid[:, None, :], (batches, MAXVIS, MAXVIS))
    result, d_tokens, grad_qkv_part, grad_out_part, gain_products = layer_core(
        local_rows, upward, allowed, wqkv, wout, gain
    )
    came = lax.all_to_all(
        jnp.take(jnp.concatenate([result, d_tokens], axis=-1), to_target, axis=0),
        "batch",
        split_axis=0,
        concat_axis=0,
        tiled=True,
    )
    came_out = came[..., :width]
    came_grad = came[..., width:]
    layer_out = jnp.take(came_out.reshape(batches * MAXVIS, width), flat_rows, axis=0)
    d_packed = jnp.take(came_grad.reshape(batches * MAXVIS, width), flat_rows, axis=0)
    partial = jnp.concatenate(
        [
            grad_qkv_part.astype(jnp.bfloat16),
            grad_out_part.astype(jnp.bfloat16),
            jnp.broadcast_to(gain_products.astype(jnp.bfloat16)[:, None], (width, 128)),
        ],
        axis=1,
    )
    summed = lax.psum_scatter(partial, "replica", scatter_dimension=0, tiled=True)
    pieces = lax.all_to_all(
        summed.reshape(batches, -1, summed.shape[1]), "batch", split_axis=0, concat_axis=0, tiled=True
    )
    reduced = jnp.sum(pieces.astype(jnp.float32), axis=0).astype(jnp.bfloat16)
    summed = lax.all_to_all(
        jnp.broadcast_to(reduced[None], (batches,) + reduced.shape),
        "batch",
        split_axis=0,
        concat_axis=0,
        tiled=True,
    )
    summed = summed.reshape(-1, summed.shape[2]).astype(jnp.float32)
    grad_q = summed[:, :qkv_cols]
    grad_o = summed[:, qkv_cols : qkv_cols + out_cols]
    grad_g = summed[:, qkv_cols + out_cols]
    return (layer_out[None], d_packed[None], grad_q, grad_o, grad_g)


def solution(mesh):
    placed = (
        P("replica", "batch", None, None),
        P("replica", "batch", None),
        P("replica", None),
        P("replica", None),
        P("replica", None),
        P("replica", None),
        P("replica"),
        P("replica", "batch", None),
    )

    return jax.shard_map(
        on_device,
        mesh=mesh,
        in_specs=placed,
        out_specs=(
            P("replica", "batch", None),
            P("replica", "batch", None),
            P("replica", None),
            P("replica", None),
            P("replica"),
        ),
        check_vma=False,
    )
```

```python
import jax
import jax.numpy as jnp
from jax import lax
from jax.sharding import PartitionSpec as P

HEADS = 16
MAXVIS = 32
MEANVIS = 16


EPS = 1e-06
NEG = -1e30


def layer_core(tokens, upward, allowed, wqkv, wout, gain):
    groups, length, width = tokens.shape
    rows = groups * length
    head_dim = width // HEADS
    scale = head_dim ** (-0.5)
    f32 = jnp.float32
    x32 = tokens.astype(jnp.float32).reshape(rows, width)
    row_average = jnp.mean(x32, axis=1, keepdims=True)
    centered_rows = x32 - row_average
    inverse_deviation = lax.rsqrt(
        jnp.mean(centered_rows * centered_rows, axis=1, keepdims=True) + EPS
    )
    standardized_rows = centered_rows * inverse_deviation
    gain_float32 = gain.astype(jnp.float32)
    layernorm_output = (standardized_rows * gain_float32).astype(jnp.bfloat16)
    qkv = jnp.dot(layernorm_output, wqkv, preferred_element_type=f32).astype(jnp.bfloat16)
    qkv = jnp.transpose(qkv.reshape(groups, length, 3, HEADS, head_dim), (2, 3, 0, 1, 4))
    query, keys, values = qkv[0], qkv[1], qkv[2]
    scores = jnp.einsum("hgqd,hgkd->hgqk", query, keys, preferred_element_type=f32) * scale
    scores = jnp.where(allowed[None], scores, NEG)
    top = jnp.max(scores, axis=-1, keepdims=True)
    expd = jnp.exp(scores - top)
    probs = expd / jnp.sum(expd, axis=-1, keepdims=True)
    weights = probs.astype(jnp.bfloat16)
    context = jnp.einsum("hgqk,hgkd->hgqd", weights, values, preferred_element_type=f32).astype(
        jnp.bfloat16
    )
    wout3 = wout.reshape(HEADS, head_dim, width)
    projected = jnp.einsum("hgqd,hde->gqe", context, wout3, preferred_element_type=f32)
    result = (x32 + projected.reshape(rows, width)).astype(jnp.bfloat16)
    up3 = upward.reshape(groups, length, width)
    d_context = jnp.einsum("gqe,hde->hgqd", up3, wout3, preferred_element_type=f32).astype(
        jnp.bfloat16
    )
    d_values = jnp.einsum(
        "hgqk,hgqd->hgkd", weights, d_context, preferred_element_type=f32
    ).astype(jnp.bfloat16)
    d_weights = jnp.einsum("hgqd,hgkd->hgqk", d_context, values, preferred_element_type=f32)
    d_scores = (
        probs * (d_weights - jnp.sum(d_weights * probs, axis=-1, keepdims=True)) * scale
    ).astype(jnp.bfloat16)
    d_query = jnp.einsum(
        "hgqk,hgkd->hgqd", d_scores, keys, preferred_element_type=f32
    ).astype(jnp.bfloat16)
    d_keys = jnp.einsum(
        "hgqk,hgqd->hgkd", d_scores, query, preferred_element_type=f32
    ).astype(jnp.bfloat16)
    d_qkv = jnp.transpose(jnp.stack([d_query, d_keys, d_values]), (2, 3, 0, 1, 4)).reshape(
        rows, 3 * width
    )
    layernorm_gradient = lax.dot_general(
        d_qkv, wqkv, (((1,), (1,)), ((), ())), preferred_element_type=f32
    )
    gain_products = jnp.sum(layernorm_gradient * standardized_rows, axis=0)
    normalized_gradient = layernorm_gradient * gain_float32
    input_gradient = inverse_deviation * (
        normalized_gradient
        - jnp.mean(normalized_gradient, axis=1, keepdims=True)
        - standardized_rows
        * jnp.mean(normalized_gradient * standardized_rows, axis=1, keepdims=True)
    )
    up_rows = upward.reshape(rows, width)
    d_tokens = (up_rows.astype(jnp.float32) + input_gradient).astype(jnp.bfloat16)
    grad_qkv_part = left_product(layernorm_output, d_qkv)
    grad_out_part = jnp.einsum(
        "hgqd,gqe->hde", context, up3, preferred_element_type=f32
    ).reshape(width, width)
    return (
        result.reshape(tokens.shape),
        d_tokens.reshape(tokens.shape),
        grad_qkv_part,
        grad_out_part,
        gain_products,
    )


def left_product(left, right):
    return lax.dot_general(
        left, right, (((0,), (0,)), ((), ())), preferred_element_type=jnp.float32
    )


def on_device(
    patches, visible_order, visible_counts, dest_rows, qkv_weight, out_weight, norm_gain, upstream
):
    qkv_cols = qkv_weight.shape[1]
    out_cols = out_weight.shape[1]
    gain_block = jnp.broadcast_to(norm_gain[:, None], (norm_gain.shape[0], 128))
    gathered = lax.all_gather(
        jnp.concatenate([qkv_weight, out_weight, gain_block], axis=1), "replica", axis=0, tiled=True
    )
    wqkv = gathered[:, :qkv_cols]
    wout = gathered[:, qkv_cols : qkv_cols + out_cols]
    gain = gathered[:, qkv_cols + out_cols]
    batches = lax.axis_size("batch")
    me_index = lax.axis_index("batch")
    cap = MEANVIS * batches
    width = wout.shape[1]
    slot = jnp.arange(MAXVIS, dtype=jnp.int32)
    sources = jnp.arange(batches, dtype=jnp.int32)
    counts_all = visible_counts[0].reshape(batches, batches)
    rows_all = dest_rows[0].reshape(batches, batches)
    mine = rows_all // cap == me_index
    src_count = jnp.sum(jnp.where(mine, counts_all, 0), axis=1)
    src_start = jnp.sum(jnp.where(mine, rows_all % cap, 0), axis=1)
    position = jnp.arange(cap, dtype=jnp.int32)
    hit = (position[:, None] >= src_start[None, :]) & (
        position[:, None] < (src_start + src_count)[None, :]
    )
    segment = jnp.sum(jnp.where(hit, sources[None, :], 0), axis=1)
    inside = jnp.sum(jnp.where(hit, position[:, None] - src_start[None, :], 0), axis=1)
    flat_rows = segment * MAXVIS + inside
    my_targets = jnp.take(rows_all, me_index, axis=0) // cap
    to_target = jnp.sum(
        jnp.where(my_targets[None, :] == sources[:, None], sources[None, :], 0), axis=1
    )
    my_counts = jnp.take(counts_all, me_index, axis=0)
    local_rows = jnp.take_along_axis(patches[0], visible_order[0, :, :MAXVIS, None], axis=1)
    live = slot[None, :] < src_count[:, None]
    pick = jnp.clip(src_start[:, None] + slot[None, :], 0, cap - 1)
    fetched = jnp.take(upstream[0], pick.reshape(-1), axis=0).reshape(batches, MAXVIS, width)
    backward_rows = jnp.where(live[..., None], fetched, jnp.zeros_like(fetched))
    returned = lax.all_to_all(backward_rows, "batch", split_axis=0, concat_axis=0, tiled=True)
    upward = jnp.take(returned, my_targets, axis=0)
    valid = slot[None, :] < my_counts[:, None]
    allowed = jnp.broadcast_to(valid[:, None, :], (batches, MAXVIS, MAXVIS))
    result, d_tokens, grad_qkv_part, grad_out_part, gain_products = layer_core(
        local_rows, upward, allowed, wqkv, wout, gain
    )
    came = lax.all_to_all(
        jnp.take(jnp.concatenate([result, d_tokens], axis=-1), to_target, axis=0),
        "batch",
        split_axis=0,
        concat_axis=0,
        tiled=True,
    )
    came_out = came[..., :width]
    came_grad = came[..., width:]
    layer_out = jnp.take(came_out.reshape(batches * MAXVIS, width), flat_rows, axis=0)
    d_packed = jnp.take(came_grad.reshape(batches * MAXVIS, width), flat_rows, axis=0)
    partial = jnp.concatenate(
        [
            grad_qkv_part.astype(jnp.bfloat16),
            grad_out_part.astype(jnp.bfloat16),
            jnp.broadcast_to(gain_products.astype(jnp.bfloat16)[:, None], (width, 128)),
        ],
        axis=1,
    )
    summed = lax.psum_scatter(partial, "replica", scatter_dimension=0, tiled=True)
    pieces = lax.all_to_all(
        summed.reshape(batches, -1, summed.shape[1]), "batch", split_axis=0, concat_axis=0, tiled=True
    )
    reduced = jnp.sum(pieces.astype(jnp.float32), axis=0).astype(jnp.bfloat16)
    summed = lax.all_to_all(
        jnp.broadcast_to(reduced[None], (batches,) + reduced.shape),
        "batch",
        split_axis=0,
        concat_axis=0,
        tiled=True,
    )
    summed = summed.reshape(-1, summed.shape[2])
    grad_q = summed[:, :qkv_cols].astype(jnp.float32)
    grad_o = summed[:, qkv_cols : qkv_cols + out_cols].astype(jnp.float32)
    grad_g = summed[:, qkv_cols + out_cols].astype(jnp.float32)
    return (layer_out[None], d_packed[None], grad_q, grad_o, grad_g)


def solution(mesh):
    placed = (
        P("replica", "batch", None, None),
        P("replica", "batch", None),
        P("replica", None),
        P("replica", None),
        P("replica", None),
        P("replica", None),
        P("replica"),
        P("replica", "batch", None),
    )

    return jax.shard_map(
        on_device,
        mesh=mesh,
        in_specs=placed,
        out_specs=(
            P("replica", "batch", None),
            P("replica", "batch", None),
            P("replica", None),
            P("replica", None),
            P("replica"),
        ),
        check_vma=False,
    )
```
